256 devices in a mesh: chain: 16 (over z_lo, y), head: 16 (over z_hi, x, core).
Axes of the slice: x: 4, y: 4, z: 8 (z_hi: 2, z_lo: 4; z = z_hi * 4 + z_lo), core: 2. Of those that a mesh axis runs over, the one named last changes fastest.
Arguments:
- signal: bfloat16 [32768, 16384], P(('chain', 'head')), may hold values from -6 to 6
- input_map: bfloat16 [32768, 2048], P(('chain', 'head')), may hold values from -0.375 to 0.375
- output_map: bfloat16 [32768, 2048], P(('chain', 'head')), may hold values from -6 to 6
- step_size: bfloat16 [32768, 256], P(('chain', 'head')), may hold values from 0.000220970869 to 1.61
- decay_rate: float32 [256], replicated, may hold values from 0.077339804 to 0.3
- skip_gain: float32 [256], replicated, may hold values from 0.5 to 1.5
Outputs:
- mixed: bfloat16 [32768, 16384], P(('chain', 'head'))
The draws below stay inside these ranges and needn't reach their ends.
All inputs are finite; a program needn't handle non-finite values.
Results may differ from the reference program's by a relative error of at most 0.0045.
Values may be sent and summed in bfloat16 or wider, within the bound.
No kernel may reach another device: no remote copies, remote signals or barrier semaphores. Data moves between devices by JAX's collectives and lax.ppermute only.
A program may use at most 192 MiB of HBM per device.

```python
from functools import partial
import jax
import jax.numpy as jnp
from jax import lax

HEADS = 256
CHANNEL_WIDTH = 64
SSTATE = 256
HEAD_GROUPS = 8
BLOCK = 256
TOKENS = 32768


def slow_heads(key):
    cutoff = 5
    return jax.random.randint(jax.random.fold_in(key, 11), (HEADS,), 0, 10) < cutoff


def head_rates(key):
    slow = slow_heads(key)
    spread = jax.random.uniform(jax.random.fold_in(key, 12), (HEADS,), jnp.float32)
    root_len = TOKENS ** 0.5
    slow_rate = (14.0 + 6.0 * spread) / root_len
    fast_rate = 0.1 + 0.2 * spread
    return (slow, jnp.where(slow, slow_rate, fast_rate).astype(jnp.float32))


def draw_decay_rate(key, part):
    slow, rates = head_rates(key)
    return rates.astype(jnp.float32)


def draw_step_size(key, part):
    slow, rates = head_rates(key)
    root_len = TOKENS ** 0.5
    fast_base = 0.1 + 0.2 * jax.random.uniform(jax.random.fold_in(key, 13), (HEADS,), jnp.float32)
    starting_shift_amount = jnp.where(slow, 0.085 / root_len, fast_base)
    approximate_guess = 0.5 + jax.random.uniform(jax.random.fold_in(key, 14), (TOKENS, HEADS), jnp.float32)
    slot_numbers = jax.random.randint(jax.random.fold_in(key, 15), (2,), 0, TOKENS)
    token_ordinal = jnp.arange(TOKENS)[:, None]
    spike_amounts = jnp.any(token_ordinal == slot_numbers[None, :], axis=1)
    impulse_signals = 1.2 + 0.4 * jax.random.uniform(jax.random.fold_in(key, 16), (TOKENS, HEADS), jnp.float32)
    impulse_signals = jnp.minimum(impulse_signals, 0.4 / rates[None, :])
    return jnp.where(spike_amounts[:, None], impulse_signals, starting_shift_amount[None, :] * approximate_guess).astype(jnp.bfloat16)


def shard_levels(own_key, extent, split, smallest, top_value):
    factor_of, own = 1.0, jax.random.fold_in(own_key, 6)
    for position, blocks in split:
        draws = jnp.exp(jax.random.uniform(jax.random.fold_in(own, position), (blocks,), jnp.float32, smallest / len(split), top_value / len(split)))
        factor_of = factor_of * jnp.repeat(draws, extent[position] // blocks).reshape([-1 if axis == position else 1 for axis in range(len(extent))])
    return factor_of


def centred(stream_key, dims, deviation, reach, split=(), dtype=jnp.bfloat16):
    level = shard_levels(stream_key, dims, split, -0.22, 0.18) if split else 1.0
    result = jax.random.normal(stream_key, dims, jnp.float32) * deviation * level
    return jnp.minimum(jnp.maximum(result, -reach), reach).astype(dtype)


def setup_inputs(seed: int = 0) -> dict:
    arg_keys = jax.random.split(jax.random.key(seed), 7)
    signal = centred(arg_keys[0], (TOKENS, HEADS * CHANNEL_WIDTH), 1.0, 6.0, ((0, 256),))
    input_map = centred(arg_keys[1], (TOKENS, HEAD_GROUPS * SSTATE), (SSTATE ** -0.5), 0.375, ((0, 256),))
    output_map = centred(arg_keys[2], (TOKENS, HEAD_GROUPS * SSTATE), 1.0, 6.0, ((0, 256),))
    step_size = draw_step_size(jax.random.fold_in(arg_keys[6], 71), 0)
    decay_rate = draw_decay_rate(jax.random.fold_in(arg_keys[6], 71), 0)
    skip_gain = jnp.clip(jax.random.uniform(arg_keys[5], (HEADS,), jnp.float32, 0.5, 1.5), 0.5, 1.5)
    return dict(signal=signal, input_map=input_map, output_map=output_map, step_size=step_size, decay_rate=decay_rate, skip_gain=skip_gain)


def block_pass(decay_rate, skip_gain, carry_state, pieces):
    signal_k, input_k, output_k, step_k = pieces
    block_len = signal_k.shape[0]
    group_heads = HEADS // HEAD_GROUPS
    step_rate = step_k.astype(jnp.float32)
    cumul = jnp.cumsum(-decay_rate[None, :] * step_rate, axis=0)
    input_groups = input_k.reshape(block_len, HEAD_GROUPS, SSTATE).astype(jnp.float32)
    output_groups = output_k.reshape(block_len, HEAD_GROUPS, SSTATE).astype(jnp.float32)
    scores = jnp.einsum("tgn,sgn->gts", output_groups, input_groups)
    scores = jnp.repeat(scores, group_heads, axis=0)
    cumul_heads = cumul.T
    causal = jnp.arange(block_len)[:, None] >= jnp.arange(block_len)[None, :]
    differ = jnp.where(causal[None], cumul_heads[:, :, None] - cumul_heads[:, None, :], 0.0)
    weights = jnp.where(causal[None], jnp.exp(differ), 0.0) * scores * step_rate.T[:, None, :]
    weights = lax.optimization_barrier(weights.astype(jnp.bfloat16)).astype(jnp.float32)
    values = signal_k.reshape(block_len, HEADS, CHANNEL_WIDTH).astype(jnp.float32)
    within = jnp.einsum("hts,shp->thp", weights, values)
    rounded = lax.optimization_barrier(carry_state.astype(jnp.bfloat16)).astype(jnp.float32)
    rounded = rounded.reshape(HEAD_GROUPS, group_heads, CHANNEL_WIDTH, SSTATE)
    carried = jnp.einsum("tgn,gjpn->tgjp", output_groups, rounded).reshape(block_len, HEADS, CHANNEL_WIDTH)
    carried = carried * jnp.exp(cumul)[:, :, None]
    mixed_out = (within + carried + skip_gain[None, :, None] * values).astype(jnp.bfloat16)
    to_end = jnp.exp(cumul[-1][None, :] - cumul) * step_rate
    update = lax.optimization_barrier((to_end[:, :, None] * values).astype(jnp.bfloat16)).astype(jnp.float32)
    update = update.reshape(block_len, HEAD_GROUPS, group_heads, CHANNEL_WIDTH)
    fresh_state = jnp.einsum("sgjp,sgn->gjpn", update, input_groups).reshape(HEADS, CHANNEL_WIDTH, SSTATE)
    new_state = jnp.exp(cumul[-1])[:, None, None] * carry_state + fresh_state
    return new_state, mixed_out.reshape(block_len, HEADS * CHANNEL_WIDTH)


def reference(signal, input_map, output_map, step_size, decay_rate, skip_gain):
    blocks = TOKENS // BLOCK
    pieces = (signal.reshape(blocks, BLOCK, HEADS * CHANNEL_WIDTH),
              input_map.reshape(blocks, BLOCK, HEAD_GROUPS * SSTATE),
              output_map.reshape(blocks, BLOCK, HEAD_GROUPS * SSTATE),
              step_size.reshape(blocks, BLOCK, HEADS))
    start_state = jnp.zeros((HEADS, CHANNEL_WIDTH, SSTATE), jnp.float32)
    final_state, result_tensors = lax.scan(partial(block_pass, decay_rate, skip_gain), start_state, pieces)
    return result_tensors.reshape(TOKENS, HEADS * CHANNEL_WIDTH)
```

```python
import jax
import jax.numpy as jnp
from jax import lax
from jax.sharding import PartitionSpec as P

HEADS = 256
CHANNEL_WIDTH = 64
SSTATE = 256
HEAD_GROUPS = 8
BLOCK = 256


def from_behind(array, axis, by):
    size = lax.axis_size(axis)
    pairs = [(i, i + by) for i in range(size) if 0 <= i + by < size]
    return lax.ppermute(array, axis, pairs)


def prepare(input_c, output_c, step_c, decay_rate, local_heads, group_count):
    chain_rows = input_c.shape[0]
    blocks = chain_rows // BLOCK
    per_group = local_heads // group_count
    head_start = lax.axis_index("head") * local_heads
    head_rates = lax.dynamic_slice_in_dim(decay_rate, head_start, local_heads)
    step_rate = step_c.astype(jnp.float32).reshape(blocks, BLOCK, local_heads)
    cumul = jnp.cumsum(-head_rates * step_rate, axis=1)
    input_groups = input_c.reshape(blocks, BLOCK, group_count, SSTATE)
    output_groups = output_c.reshape(blocks, BLOCK, group_count, SSTATE)
    causal = jnp.arange(BLOCK)[:, None] >= jnp.arange(BLOCK)[None, :]

    def block_weights(pieces):
        cumul_k, step_k, input_k, output_k = pieces
        scores = jnp.einsum("tgn,sgn->gts", output_k, input_k, preferred_element_type=jnp.float32)
        cumul_heads = cumul_k.T.reshape(group_count, per_group, BLOCK)
        differ = jnp.where(causal, cumul_heads[:, :, :, None] - cumul_heads[:, :, None, :], 0.0)
        decays = jnp.where(causal, jnp.exp(differ), 0.0)
        step_heads = step_k.T.reshape(group_count, per_group, 1, BLOCK)
        weights = decays * scores[:, None] * step_heads
        return weights.astype(jnp.bfloat16).reshape(local_heads, BLOCK, BLOCK)

    weights = lax.map(block_weights, (cumul, step_rate, input_groups, output_groups))
    return (step_rate, cumul, input_groups, output_groups, weights)


def finish(signal_c, prepared, skip_gain, local_heads, group_count):
    step_rate, cumul, input_groups, output_groups, weights = prepared
    blocks = cumul.shape[0]
    per_group = local_heads // group_count
    values = signal_c.reshape(blocks, BLOCK, local_heads, CHANNEL_WIDTH)
    values_wide = values.astype(jnp.float32)
    within = jnp.einsum("khts,kshp->kthp", weights, values, preferred_element_type=jnp.float32)
    to_end = jnp.exp(cumul[:, -1:, :] - cumul) * step_rate
    update = (to_end[..., None] * values_wide).astype(jnp.bfloat16)
    update = update.reshape(blocks, BLOCK, group_count, per_group, CHANNEL_WIDTH)
    fresh_state = jnp.einsum(
        "ksgjp,ksgn->kgjpn", update, input_groups, preferred_element_type=jnp.float32
    )
    fresh_state = fresh_state.reshape(blocks, local_heads, CHANNEL_WIDTH, SSTATE)
    block_ends = cumul[:, -1, :]

    def carry_step(carry_state, pieces):
        block_end, fresh_block = pieces
        return (jnp.exp(block_end)[:, None, None] * carry_state + fresh_block, carry_state)

    empty_state = jnp.zeros((local_heads, CHANNEL_WIDTH, SSTATE), jnp.float32)
    final_state, starts = lax.scan(carry_step, empty_state, (block_ends, fresh_state))
    before = jnp.cumsum(block_ends, axis=0) - block_ends
    totals = jnp.sum(block_ends, axis=0)
    chain_len = lax.axis_size("chain")
    own_decay = jnp.exp(totals)
    got_decay = from_behind(own_decay, "chain", 1)
    got_state = from_behind(final_state, "chain", 1)
    span_decay = got_decay * own_decay
    span_state = own_decay[:, None, None] * got_state + final_state
    incoming_state = got_state
    incoming_decay = got_decay
    shift = 2
    while shift < chain_len:
        got_decay = from_behind(span_decay, "chain", shift)
        got_state = from_behind(span_state, "chain", shift)
        incoming_state = incoming_decay[:, None, None] * got_state + incoming_state
        incoming_decay = incoming_decay * got_decay
        if 2 * shift < chain_len:
            span_state = span_decay[:, None, None] * got_state + span_state
            span_decay = span_decay * got_decay
        shift *= 2
    starts = starts + jnp.exp(before)[:, :, None, None] * incoming_state
    rounded = starts.astype(jnp.bfloat16).reshape(
        blocks, group_count, per_group, CHANNEL_WIDTH, SSTATE
    )
    carried = jnp.einsum(
        "ktgn,kgjpn->ktgjp", output_groups, rounded, preferred_element_type=jnp.float32
    )
    carried = carried.reshape(blocks, BLOCK, local_heads, CHANNEL_WIDTH) * jnp.exp(cumul)[..., None]
    head_start = lax.axis_index("head") * local_heads
    gain_heads = lax.dynamic_slice_in_dim(skip_gain, head_start, local_heads)
    result = (within + carried + gain_heads[:, None] * values_wide).astype(jnp.bfloat16)
    result = result.reshape(blocks * BLOCK, local_heads * CHANNEL_WIDTH)
    return lax.all_to_all(result, "head", split_axis=0, concat_axis=1, tiled=True)


def shards(signal, input_map, output_map, step_size, decay_rate, skip_gain):
    head_count = lax.axis_size("head")
    local_heads = HEADS // head_count
    group_heads = HEADS // HEAD_GROUPS
    group_count = max(1, local_heads // group_heads)
    copies = max(1, group_heads // local_heads)
    row_count = signal.shape[0]
    input_rep = jnp.repeat(
        input_map.reshape(row_count, HEAD_GROUPS, SSTATE), copies, axis=1
    ).reshape(row_count, -1)
    output_rep = jnp.repeat(
        output_map.reshape(row_count, HEAD_GROUPS, SSTATE), copies, axis=1
    ).reshape(row_count, -1)
    signal_c, input_c, output_c, step_c = (
        lax.all_to_all(signal, "head", split_axis=1, concat_axis=0, tiled=True),
        lax.all_to_all(input_rep, "head", split_axis=1, concat_axis=0, tiled=True),
        lax.all_to_all(output_rep, "head", split_axis=1, concat_axis=0, tiled=True),
        lax.all_to_all(step_size, "head", split_axis=1, concat_axis=0, tiled=True),
    )
    prepared = prepare(input_c, output_c, step_c, decay_rate, local_heads, group_count)
    return finish(signal_c, prepared, skip_gain, local_heads, group_count)


def solution(mesh):
    return jax.shard_map(
        shards,
        mesh=mesh,
        in_specs=(
            P(("chain", "head"), None),
            P(("chain", "head"), None),
            P(("chain", "head"), None),
            P(("chain", "head"), None),
            P(),
            P(),
        ),
        out_specs=P(("chain", "head"), None),
        check_vma=False,
    )
```

```python
import jax
import jax.numpy as jnp
from jax import lax
from jax.sharding import PartitionSpec as P

HEADS = 256
CHANNEL_WIDTH = 64
SSTATE = 256
HEAD_GROUPS = 8
BLOCK = 256


def from_behind(array, axis, by):
    size = lax.axis_size(axis)
    pairs = [(i, i + by) for i in range(size) if 0 <= i + by < size]
    return lax.ppermute(array, axis, pairs)


def prepare(input_c, output_c, step_c, decay_rate, local_heads, group_count):
    chain_rows = input_c.shape[0]
    blocks = chain_rows // BLOCK
    per_group = local_heads // group_count
    head_start = lax.axis_index("head") * local_heads
    head_rates = lax.dynamic_slice_in_dim(decay_rate, head_start, local_heads)
    step_rate = step_c.astype(jnp.float32).reshape(blocks, BLOCK, local_heads)
    cumul = jnp.cumsum(-head_rates * step_rate, axis=1)
    input_groups = input_c.reshape(blocks, BLOCK, group_count, SSTATE)
    output_groups = output_c.reshape(blocks, BLOCK, group_count, SSTATE)
    causal = jnp.arange(BLOCK)[:, None] >= jnp.arange(BLOCK)[None, :]

    def block_weights(pieces):
        cumul_k, step_k, input_k, output_k = pieces
        scores = jnp.einsum("tgn,sgn->gts", output_k, input_k, preferred_element_type=jnp.float32)
        cumul_heads = cumul_k.T.reshape(group_count, per_group, BLOCK)
        differ = jnp.where(causal, cumul_heads[:, :, :, None] - cumul_heads[:, :, None, :], 0.0)
        decays = jnp.where(causal, jnp.exp(differ), 0.0)
        step_heads = step_k.T.reshape(group_count, per_group, 1, BLOCK)
        weights = decays * scores[:, None] * step_heads
        return weights.astype(jnp.bfloat16).reshape(local_heads, BLOCK, BLOCK)

    weights = lax.map(block_weights, (cumul, step_rate, input_groups, output_groups))
    return (step_rate, cumul, input_groups, output_groups, weights)


def finish(signal_c, prepared, skip_gain, local_heads, group_count):
    step_rate, cumul, input_groups, output_groups, weights = prepared
    blocks = cumul.shape[0]
    per_group = local_heads // group_count
    values = signal_c.reshape(blocks, BLOCK, local_heads, CHANNEL_WIDTH)
    values_wide = values.astype(jnp.float32)
    within = jnp.einsum("khts,kshp->kthp", weights, values, preferred_element_type=jnp.float32)
    to_end = jnp.exp(cumul[:, -1:, :] - cumul) * step_rate
    update = (to_end[..., None] * values_wide).astype(jnp.bfloat16)
    update = update.reshape(blocks, BLOCK, group_count, per_group, CHANNEL_WIDTH)
    fresh_state = jnp.einsum(
        "ksgjp,ksgn->kgjpn", update, input_groups, preferred_element_type=jnp.float32
    )
    fresh_state = fresh_state.reshape(blocks, local_heads, CHANNEL_WIDTH, SSTATE)
    block_ends = cumul[:, -1, :]

    def carry_step(carry_state, pieces):
        block_end, fresh_block = pieces
        return (jnp.exp(block_end)[:, None, None] * carry_state + fresh_block, carry_state)

    empty_state = jnp.zeros((local_heads, CHANNEL_WIDTH, SSTATE), jnp.float32)
    final_state, starts = lax.scan(carry_step, empty_state, (block_ends, fresh_state))
    before = jnp.cumsum(block_ends, axis=0) - block_ends
    totals = jnp.sum(block_ends, axis=0)
    chain_len = lax.axis_size("chain")
    chain_pos = lax.axis_index("chain")
    shard_totals = lax.all_gather(totals, "chain")
    order = jnp.arange(chain_len)

    def span_decay(first, last):
        inside = (order >= first) & (order <= last)
        return jnp.exp(jnp.sum(jnp.where(inside[:, None], shard_totals, 0.0), axis=0))

    got_state = from_behind(final_state, "chain", 1)
    span_state = jnp.exp(totals)[:, None, None] * got_state + final_state
    incoming_state = got_state
    shift = 2
    while shift < chain_len:
        got_state = from_behind(span_state, "chain", shift)
        incoming_decay = span_decay(chain_pos - shift + 1, chain_pos - 1)
        incoming_state = incoming_decay[:, None, None] * got_state + incoming_state
        if 2 * shift < chain_len:
            own_decay = span_decay(chain_pos - shift + 1, chain_pos)
            span_state = own_decay[:, None, None] * got_state + span_state
        shift *= 2
    starts = starts + jnp.exp(before)[:, :, None, None] * incoming_state
    rounded = starts.astype(jnp.bfloat16).reshape(
        blocks, group_count, per_group, CHANNEL_WIDTH, SSTATE
    )
    carried = jnp.einsum(
        "ktgn,kgjpn->ktgjp", output_groups, rounded, preferred_element_type=jnp.float32
    )
    carried = carried.reshape(blocks, BLOCK, local_heads, CHANNEL_WIDTH) * jnp.exp(cumul)[..., None]
    head_start = lax.axis_index("head") * local_heads
    gain_heads = lax.dynamic_slice_in_dim(skip_gain, head_start, local_heads)
    result = (within + carried + gain_heads[:, None] * values_wide).astype(jnp.bfloat16)
    head_count = lax.axis_size("head")
    result = result.reshape(head_count, -1, local_heads * CHANNEL_WIDTH).transpose(1, 0, 2)
    result = lax.all_to_all(result, "head", split_axis=1, concat_axis=1, tiled=True)
    return result.reshape(result.shape[0], -1)


def shards(signal, input_map, output_map, step_size, decay_rate, skip_gain):
    head_count = lax.axis_size("head")
    local_heads = HEADS // head_count
    group_heads = HEADS // HEAD_GROUPS
    group_count = max(1, local_heads // group_heads)
    copies = max(1, group_heads // local_heads)
    row_count = signal.shape[0]
    input_rep = jnp.repeat(
        input_map.reshape(row_count, HEAD_GROUPS, SSTATE), copies, axis=1
    ).reshape(row_count, -1)
    output_rep = jnp.repeat(
        output_map.reshape(row_count, HEAD_GROUPS, SSTATE), copies, axis=1
    ).reshape(row_count, -1)
    signal_c, input_c, output_c, step_c = (
        lax.all_to_all(signal, "head", split_axis=1, concat_axis=0, tiled=True),
        lax.all_to_all(input_rep, "head", split_axis=1, concat_axis=0, tiled=True),
        lax.all_to_all(output_rep, "head", split_axis=1, concat_axis=0, tiled=True),
        lax.all_to_all(step_size, "head", split_axis=1, concat_axis=0, tiled=True),
    )
    prepared = prepare(input_c, output_c, step_c, decay_rate, local_heads, group_count)
    return finish(signal_c, prepared, skip_gain, local_heads, group_count)


def solution(mesh):
    return jax.shard_map(
        shards,
        mesh=mesh,
        in_specs=(
            P(("chain", "head"), None),
            P(("chain", "head"), None),
            P(("chain", "head"), None),
            P(("chain", "head"), None),
            P(),
            P(),
        ),
        out_specs=P(("chain", "head"), None),
        check_vma=False,
    )
```

```python
import jax
import jax.numpy as jnp
from jax import lax
from jax.sharding import PartitionSpec as P

HEADS = 256
CHANNEL_WIDTH = 64
SSTATE = 256
HEAD_GROUPS = 8
BLOCK = 256


def from_behind(array, axis, by):
    size = lax.axis_size(axis)
    pairs = [(i, i + by) for i in range(size) if 0 <= i + by < size]
    return lax.ppermute(array, axis, pairs)


def prepare(input_c, output_c, step_c, decay_rate, local_heads, group_count):
    chain_rows = input_c.shape[0]
    blocks = chain_rows // BLOCK
    per_group = local_heads // group_count
    head_start = lax.axis_index("head") * local_heads
    head_rates = lax.dynamic_slice_in_dim(decay_rate, head_start, local_heads)
    step_rate = step_c.astype(jnp.float32).reshape(blocks, BLOCK, local_heads)
    cumul = jnp.cumsum(-head_rates * step_rate, axis=1)
    input_groups = input_c.reshape(blocks, BLOCK, group_count, SSTATE)
    output_groups = output_c.reshape(blocks, BLOCK, group_count, SSTATE)
    causal = jnp.arange(BLOCK)[:, None] >= jnp.arange(BLOCK)[None, :]

    def block_weights(pieces):
        cumul_k, step_k, input_k, output_k = pieces
        scores = jnp.einsum("tgn,sgn->gts", output_k, input_k, preferred_element_type=jnp.float32)
        cumul_heads = cumul_k.T.reshape(group_count, per_group, BLOCK)
        differ = jnp.where(causal, cumul_heads[:, :, :, None] - cumul_heads[:, :, None, :], 0.0)
        decays = jnp.where(causal, jnp.exp(differ), 0.0)
        step_heads = step_k.T.reshape(group_count, per_group, 1, BLOCK)
        weights = decays * scores[:, None] * step_heads
        return weights.astype(jnp.bfloat16).reshape(local_heads, BLOCK, BLOCK)

    weights = lax.map(block_weights, (cumul, step_rate, input_groups, output_groups))
    return (step_rate, cumul, input_groups, output_groups, weights)


def finish(signal_c, prepared, skip_gain, local_heads, group_count):
    step_rate, cumul, input_groups, output_groups, weights = prepared
    blocks = cumul.shape[0]
    per_group = local_heads // group_count
    values = signal_c.reshape(blocks, BLOCK, local_heads, CHANNEL_WIDTH)
    values_wide = values.astype(jnp.float32)
    within = jnp.einsum("khts,kshp->kthp", weights, values, preferred_element_type=jnp.float32)
    to_end = jnp.exp(cumul[:, -1:, :] - cumul) * step_rate
    update = (to_end[..., None] * values_wide).astype(jnp.bfloat16)
    update = update.reshape(blocks, BLOCK, group_count, per_group, CHANNEL_WIDTH)
    fresh_state = jnp.einsum(
        "ksgjp,ksgn->kgjpn", update, input_groups, preferred_element_type=jnp.float32
    )
    fresh_state = fresh_state.reshape(blocks, local_heads, CHANNEL_WIDTH, SSTATE)
    block_ends = cumul[:, -1, :]

    def carry_step(carry_state, pieces):
        block_end, fresh_block = pieces
        return (jnp.exp(block_end)[:, None, None] * carry_state + fresh_block, carry_state)

    empty_state = jnp.zeros((local_heads, CHANNEL_WIDTH, SSTATE), jnp.float32)
    final_state, starts = lax.scan(carry_step, empty_state, (block_ends, fresh_state))
    before = jnp.cumsum(block_ends, axis=0) - block_ends
    totals = jnp.sum(block_ends, axis=0)
    chain_len = lax.axis_size("chain")
    state_rows = local_heads * CHANNEL_WIDTH

    def pack(decay, state):
        decay_row = jnp.broadcast_to(decay[None, :], (8, local_heads))
        decay_row = jnp.pad(decay_row, ((0, 0), (0, SSTATE - local_heads)))
        return jnp.concatenate([state.reshape(state_rows, SSTATE), decay_row], axis=0)

    def unpack(packed):
        state = packed[:state_rows].reshape(local_heads, CHANNEL_WIDTH, SSTATE)
        return packed[state_rows, :local_heads], state

    own_decay = jnp.exp(totals)
    got_decay, got_state = unpack(from_behind(pack(own_decay, final_state), "chain", 1))
    span_decay = got_decay * own_decay
    span_state = own_decay[:, None, None] * got_state + final_state
    incoming_state = got_state
    incoming_decay = got_decay
    shift = 2
    while shift < chain_len:
        got_decay, got_state = unpack(from_behind(pack(span_decay, span_state), "chain", shift))
        incoming_state = incoming_decay[:, None, None] * got_state + incoming_state
        incoming_decay = incoming_decay * got_decay
        if 2 * shift < chain_len:
            span_state = span_decay[:, None, None] * got_state + span_state
            span_decay = span_decay * got_decay
        shift *= 2
    starts = starts + jnp.exp(before)[:, :, None, None] * incoming_state
    rounded = starts.astype(jnp.bfloat16).reshape(
        blocks, group_count, per_group, CHANNEL_WIDTH, SSTATE
    )
    carried = jnp.einsum(
        "ktgn,kgjpn->ktgjp", output_groups, rounded, preferred_element_type=jnp.float32
    )
    carried = carried.reshape(blocks, BLOCK, local_heads, CHANNEL_WIDTH) * jnp.exp(cumul)[..., None]
    head_start = lax.axis_index("head") * local_heads
    gain_heads = lax.dynamic_slice_in_dim(skip_gain, head_start, local_heads)
    result = (within + carried + gain_heads[:, None] * values_wide).astype(jnp.bfloat16)
    head_count = lax.axis_size("head")
    result = result.reshape(head_count, -1, local_heads * CHANNEL_WIDTH).transpose(1, 0, 2)
    result = lax.all_to_all(result, "head", split_axis=1, concat_axis=1, tiled=True)
    return result.reshape(result.shape[0], -1)


def shards(signal, input_map, output_map, step_size, decay_rate, skip_gain):
    head_count = lax.axis_size("head")
    local_heads = HEADS // head_count
    group_heads = HEADS // HEAD_GROUPS
    group_count = max(1, local_heads // group_heads)
    copies = max(1, group_heads // local_heads)
    row_count = signal.shape[0]
    input_rep = jnp.repeat(
        input_map.reshape(row_count, HEAD_GROUPS, SSTATE), copies, axis=1
    ).reshape(row_count, -1)
    output_rep = jnp.repeat(
        output_map.reshape(row_count, HEAD_GROUPS, SSTATE), copies, axis=1
    ).reshape(row_count, -1)
    signal_c, input_c, output_c, step_c = (
        lax.all_to_all(signal, "head", split_axis=1, concat_axis=0, tiled=True),
        lax.all_to_all(input_rep, "head", split_axis=1, concat_axis=0, tiled=True),
        lax.all_to_all(output_rep, "head", split_axis=1, concat_axis=0, tiled=True),
        lax.all_to_all(step_size, "head", split_axis=1, concat_axis=0, tiled=True),
    )
    prepared = prepare(input_c, output_c, step_c, decay_rate, local_heads, group_count)
    return finish(signal_c, prepared, skip_gain, local_heads, group_count)


def solution(mesh):
    return jax.shard_map(
        shards,
        mesh=mesh,
        in_specs=(
            P(("chain", "head"), None),
            P(("chain", "head"), None),
            P(("chain", "head"), None),
            P(("chain", "head"), None),
            P(),
            P(),
        ),
        out_specs=P(("chain", "head"), None),
        check_vma=False,
    )
```

```python
import jax
import jax.numpy as jnp
from jax import lax
from jax.sharding import PartitionSpec as P

HEADS = 256
CHANNEL_WIDTH = 64
SSTATE = 256
HEAD_GROUPS = 8
BLOCK = 256


SEQ = ("chain", "half")
LANE = "lane"


def from_behind(array, axis, by):
    size = lax.psum(1, axis)
    pairs = [(i, i + by) for i in range(size) if 0 <= i + by < size]
    return lax.ppermute(array, axis, pairs)


def prepare(input_c, output_c, step_c, decay_rate, local_heads, group_count):
    chain_rows = input_c.shape[0]
    blocks = chain_rows // BLOCK
    per_group = local_heads // group_count
    head_start = lax.axis_index(LANE) * local_heads
    head_rates = lax.dynamic_slice_in_dim(decay_rate, head_start, local_heads)
    step_rate = step_c.astype(jnp.float32).reshape(blocks, BLOCK, local_heads)
    cumul = jnp.cumsum(-head_rates * step_rate, axis=1)
    input_groups = input_c.reshape(blocks, BLOCK, group_count, SSTATE)
    output_groups = output_c.reshape(blocks, BLOCK, group_count, SSTATE)
    causal = jnp.arange(BLOCK)[:, None] >= jnp.arange(BLOCK)[None, :]

    def block_weights(pieces):
        cumul_k, step_k, input_k, output_k = pieces
        scores = jnp.einsum("tgn,sgn->gts", output_k, input_k, preferred_element_type=jnp.float32)
        cumul_heads = cumul_k.T.reshape(group_count, per_group, BLOCK)
        differ = jnp.where(causal, cumul_heads[:, :, :, None] - cumul_heads[:, :, None, :], 0.0)
        decays = jnp.where(causal, jnp.exp(differ), 0.0)
        step_heads = step_k.T.reshape(group_count, per_group, 1, BLOCK)
        weights = decays * scores[:, None] * step_heads
        return weights.astype(jnp.bfloat16).reshape(local_heads, BLOCK, BLOCK)

    weights = lax.map(block_weights, (cumul, step_rate, input_groups, output_groups))
    return (step_rate, cumul, input_groups, output_groups, weights)


def finish(signal_c, prepared, skip_gain, local_heads, group_count):
    step_rate, cumul, input_groups, output_groups, weights = prepared
    blocks = cumul.shape[0]
    per_group = local_heads // group_count
    values = signal_c.reshape(blocks, BLOCK, local_heads, CHANNEL_WIDTH)
    values_wide = values.astype(jnp.float32)
    within = jnp.einsum("khts,kshp->kthp", weights, values, preferred_element_type=jnp.float32)
    to_end = jnp.exp(cumul[:, -1:, :] - cumul) * step_rate
    update = (to_end[..., None] * values_wide).astype(jnp.bfloat16)
    update = update.reshape(blocks, BLOCK, group_count, per_group, CHANNEL_WIDTH)
    fresh_state = jnp.einsum(
        "ksgjp,ksgn->kgjpn", update, input_groups, preferred_element_type=jnp.float32
    )
    fresh_state = fresh_state.reshape(blocks, local_heads, CHANNEL_WIDTH, SSTATE)
    block_ends = cumul[:, -1, :]

    def carry_step(carry_state, pieces):
        block_end, fresh_block = pieces
        return (jnp.exp(block_end)[:, None, None] * carry_state + fresh_block, carry_state)

    empty_state = jnp.zeros((local_heads, CHANNEL_WIDTH, SSTATE), jnp.float32)
    final_state, starts = lax.scan(carry_step, empty_state, (block_ends, fresh_state))
    before = jnp.cumsum(block_ends, axis=0) - block_ends
    totals = jnp.sum(block_ends, axis=0)
    chain_len = lax.psum(1, SEQ)
    state_rows = local_heads * CHANNEL_WIDTH

    def pack(decay, state):
        decay_row = jnp.broadcast_to(decay[None, :], (8, local_heads))
        decay_row = jnp.pad(decay_row, ((0, 0), (0, SSTATE - local_heads)))
        return jnp.concatenate([state.reshape(state_rows, SSTATE), decay_row], axis=0)

    def unpack(packed):
        state = packed[:state_rows].reshape(local_heads, CHANNEL_WIDTH, SSTATE)
        return packed[state_rows, :local_heads], state

    own_decay = jnp.exp(totals)
    got_decay, got_state = unpack(from_behind(pack(own_decay, final_state), SEQ, 1))
    span_decay = got_decay * own_decay
    span_state = own_decay[:, None, None] * got_state + final_state
    incoming_state = got_state
    incoming_decay = got_decay
    shift = 2
    while shift < chain_len:
        got_decay, got_state = unpack(from_behind(pack(span_decay, span_state), SEQ, shift))
        incoming_state = incoming_decay[:, None, None] * got_state + incoming_state
        incoming_decay = incoming_decay * got_decay
        if 2 * shift < chain_len:
            span_state = span_decay[:, None, None] * got_state + span_state
            span_decay = span_decay * got_decay
        shift *= 2
    starts = starts + jnp.exp(before)[:, :, None, None] * incoming_state
    rounded = starts.astype(jnp.bfloat16).reshape(
        blocks, group_count, per_group, CHANNEL_WIDTH, SSTATE
    )
    carried = jnp.einsum(
        "ktgn,kgjpn->ktgjp", output_groups, rounded, preferred_element_type=jnp.float32
    )
    carried = carried.reshape(blocks, BLOCK, local_heads, CHANNEL_WIDTH) * jnp.exp(cumul)[..., None]
    head_start = lax.axis_index(LANE) * local_heads
    gain_heads = lax.dynamic_slice_in_dim(skip_gain, head_start, local_heads)
    result = (within + carried + gain_heads[:, None] * values_wide).astype(jnp.bfloat16)
    head_count = lax.axis_size(LANE)
    result = result.reshape(head_count, -1, local_heads * CHANNEL_WIDTH).transpose(1, 0, 2)
    result = lax.all_to_all(result, LANE, split_axis=1, concat_axis=1, tiled=True)
    return result.reshape(result.shape[0], -1)


def shards(signal, input_map, output_map, step_size, decay_rate, skip_gain):
    head_count = lax.axis_size(LANE)
    local_heads = HEADS // head_count
    group_heads = HEADS // HEAD_GROUPS
    group_count = max(1, local_heads // group_heads)
    copies = max(1, group_heads // local_heads)
    row_count = signal.shape[0]
    input_rep = jnp.repeat(
        input_map.reshape(row_count, HEAD_GROUPS, SSTATE), copies, axis=1
    ).reshape(row_count, -1)
    output_rep = jnp.repeat(
        output_map.reshape(row_count, HEAD_GROUPS, SSTATE), copies, axis=1
    ).reshape(row_count, -1)
    signal_c, input_c, output_c, step_c = (
        lax.all_to_all(signal, LANE, split_axis=1, concat_axis=0, tiled=True),
        lax.all_to_all(input_rep, LANE, split_axis=1, concat_axis=0, tiled=True),
        lax.all_to_all(output_rep, LANE, split_axis=1, concat_axis=0, tiled=True),
        lax.all_to_all(step_size, LANE, split_axis=1, concat_axis=0, tiled=True),
    )
    prepared = prepare(input_c, output_c, step_c, decay_rate, local_heads, group_count)
    return finish(signal_c, prepared, skip_gain, local_heads, group_count)


def solution(mesh):
    chain_count, head_count = mesh.devices.shape
    halves = 2 if head_count % 2 == 0 else 1
    split_mesh = jax.sharding.Mesh(
        mesh.devices.reshape(chain_count, halves, head_count // halves), ("chain", "half", LANE)
    )
    rows = P(("chain", "half", LANE), None)
    return jax.shard_map(
        shards,
        mesh=split_mesh,
        in_specs=(rows, rows, rows, rows, P(), P()),
        out_specs=rows,
        check_vma=False,
    )
```

```python
import jax
import jax.numpy as jnp
from jax import lax
from jax.sharding import PartitionSpec as P

HEADS = 256
CHANNEL_WIDTH = 64
SSTATE = 256
HEAD_GROUPS = 8
BLOCK = 256


SEQ = ("chain", "half")
LANE = "lane"


def from_behind(array, axis, by):
    size = lax.psum(1, axis)
    pairs = [(i, i + by) for i in range(size) if 0 <= i + by < size]
    return lax.ppermute(array, axis, pairs)


def prepare(input_c, output_c, step_c, decay_rate, local_heads, group_count):
    chain_rows = input_c.shape[0]
    blocks = chain_rows // BLOCK
    per_group = local_heads // group_count
    head_start = lax.axis_index(LANE) * local_heads
    head_rates = lax.dynamic_slice_in_dim(decay_rate, head_start, local_heads)
    step_rate = step_c.astype(jnp.float32).reshape(blocks, BLOCK, local_heads)
    cumul = jnp.cumsum(-head_rates * step_rate, axis=1)
    input_groups = input_c.reshape(blocks, BLOCK, group_count, SSTATE)
    output_groups = output_c.reshape(blocks, BLOCK, group_count, SSTATE)
    causal = jnp.arange(BLOCK)[:, None] >= jnp.arange(BLOCK)[None, :]

    def block_weights(pieces):
        cumul_k, step_k, input_k, output_k = pieces
        scores = jnp.einsum("tgn,sgn->gts", output_k, input_k, preferred_element_type=jnp.float32)
        cumul_heads = cumul_k.T.reshape(group_count, per_group, BLOCK)
        differ = jnp.where(causal, cumul_heads[:, :, :, None] - cumul_heads[:, :, None, :], 0.0)
        decays = jnp.where(causal, jnp.exp(differ), 0.0)
        step_heads = step_k.T.reshape(group_count, per_group, 1, BLOCK)
        weights = decays * scores[:, None] * step_heads
        return weights.astype(jnp.bfloat16).reshape(local_heads, BLOCK, BLOCK)

    weights = lax.map(block_weights, (cumul, step_rate, input_groups, output_groups))
    return (step_rate, cumul, input_groups, output_groups, weights)


def finish(signal_c, prepared, skip_gain, local_heads, group_count):
    step_rate, cumul, input_groups, output_groups, weights = prepared
    blocks = cumul.shape[0]
    per_group = local_heads // group_count
    values = signal_c.reshape(blocks, BLOCK, local_heads, CHANNEL_WIDTH)
    values_wide = values.astype(jnp.float32)
    within = jnp.einsum("khts,kshp->kthp", weights, values, preferred_element_type=jnp.float32)
    to_end = jnp.exp(cumul[:, -1:, :] - cumul) * step_rate
    update = (to_end[..., None] * values_wide).astype(jnp.bfloat16)
    update = update.reshape(blocks, BLOCK, group_count, per_group, CHANNEL_WIDTH)
    fresh_state = jnp.einsum(
        "ksgjp,ksgn->kgjpn", update, input_groups, preferred_element_type=jnp.float32
    )
    fresh_state = fresh_state.reshape(blocks, local_heads, CHANNEL_WIDTH, SSTATE)
    block_ends = cumul[:, -1, :]

    def carry_step(carry_state, pieces):
        block_end, fresh_block = pieces
        return (jnp.exp(block_end)[:, None, None] * carry_state + fresh_block, carry_state)

    empty_state = jnp.zeros((local_heads, CHANNEL_WIDTH, SSTATE), jnp.float32)
    final_state, starts = lax.scan(carry_step, empty_state, (block_ends, fresh_state))
    before = jnp.cumsum(block_ends, axis=0) - block_ends
    totals = jnp.sum(block_ends, axis=0)
    chain_len = lax.axis_size("chain")
    half_count = lax.axis_size("half")
    part = local_heads // half_count
    half = lax.axis_index("half")

    def pack(decay, state):
        rows = state.shape[0] * CHANNEL_WIDTH
        decay_row = jnp.broadcast_to(decay[None, :], (8, decay.shape[0]))
        decay_row = jnp.pad(decay_row, ((0, 0), (0, SSTATE - decay.shape[0])))
        return jnp.concatenate([state.reshape(rows, SSTATE), decay_row], axis=0)

    def unpack(packed, heads, decays):
        rows = heads * CHANNEL_WIDTH
        state = packed[:rows].reshape(heads, CHANNEL_WIDTH, SSTATE)
        return packed[rows, :decays], state

    def heads_of(array, which):
        return lax.dynamic_slice_in_dim(array, which * part, part)

    def swap(array):
        return lax.ppermute(array, "half", [(0, 1), (1, 0)])

    own_decay = jnp.exp(totals)
    if half_count == 2:
        sent = pack(own_decay, heads_of(final_state, 1 - half))
        other_decay, other_state = unpack(swap(sent), part, local_heads)
        mine_state = heads_of(final_state, half)
        first = half == 0
        first_decay = jnp.where(first, own_decay, other_decay)
        second_decay = jnp.where(first, other_decay, own_decay)
        first_state = jnp.where(first, mine_state, other_state)
        second_state = jnp.where(first, other_state, mine_state)
        link_decay = heads_of(first_decay * second_decay, half)
        link_state = heads_of(second_decay, half)[:, None, None] * first_state + second_state
    else:
        link_decay, link_state = own_decay, final_state

    got_decay, got_state = unpack(
        from_behind(pack(link_decay, link_state), "chain", 1), part, part
    )
    span_decay = got_decay * link_decay
    span_state = link_decay[:, None, None] * got_state + link_state
    incoming_state = got_state
    incoming_decay = got_decay
    shift = 2
    while shift < chain_len:
        got_decay, got_state = unpack(
            from_behind(pack(span_decay, span_state), "chain", shift), part, part
        )
        incoming_state = incoming_decay[:, None, None] * got_state + incoming_state
        incoming_decay = incoming_decay * got_decay
        if 2 * shift < chain_len:
            span_state = span_decay[:, None, None] * got_state + span_state
            span_decay = span_decay * got_decay
        shift *= 2

    if half_count == 2:
        into_second = heads_of(first_decay, half)[:, None, None] * incoming_state + first_state
        mine_start = jnp.where(first, incoming_state, into_second)
        other_start = swap(jnp.where(first, into_second, incoming_state))
        incoming_state = jnp.where(
            first,
            jnp.concatenate([mine_start, other_start], axis=0),
            jnp.concatenate([other_start, mine_start], axis=0),
        )
    starts = starts + jnp.exp(before)[:, :, None, None] * incoming_state
    rounded = starts.astype(jnp.bfloat16).reshape(
        blocks, group_count, per_group, CHANNEL_WIDTH, SSTATE
    )
    carried = jnp.einsum(
        "ktgn,kgjpn->ktgjp", output_groups, rounded, preferred_element_type=jnp.float32
    )
    carried = carried.reshape(blocks, BLOCK, local_heads, CHANNEL_WIDTH) * jnp.exp(cumul)[..., None]
    head_start = lax.axis_index(LANE) * local_heads
    gain_heads = lax.dynamic_slice_in_dim(skip_gain, head_start, local_heads)
    result = (within + carried + gain_heads[:, None] * values_wide).astype(jnp.bfloat16)
    head_count = lax.axis_size(LANE)
    result = result.reshape(head_count, -1, local_heads * CHANNEL_WIDTH).transpose(1, 0, 2)
    result = lax.all_to_all(result, LANE, split_axis=1, concat_axis=1, tiled=True)
    return result.reshape(result.shape[0], -1)


def shards(signal, input_map, output_map, step_size, decay_rate, skip_gain):
    head_count = lax.axis_size(LANE)
    local_heads = HEADS // head_count
    group_heads = HEADS // HEAD_GROUPS
    group_count = max(1, local_heads // group_heads)
    copies = max(1, group_heads // local_heads)
    row_count = signal.shape[0]
    input_rep = jnp.repeat(
        input_map.reshape(row_count, HEAD_GROUPS, SSTATE), copies, axis=1
    ).reshape(row_count, -1)
    output_rep = jnp.repeat(
        output_map.reshape(row_count, HEAD_GROUPS, SSTATE), copies, axis=1
    ).reshape(row_count, -1)
    signal_c, input_c, output_c, step_c = (
        lax.all_to_all(signal, LANE, split_axis=1, concat_axis=0, tiled=True),
        lax.all_to_all(input_rep, LANE, split_axis=1, concat_axis=0, tiled=True),
        lax.all_to_all(output_rep, LANE, split_axis=1, concat_axis=0, tiled=True),
        lax.all_to_all(step_size, LANE, split_axis=1, concat_axis=0, tiled=True),
    )
    prepared = prepare(input_c, output_c, step_c, decay_rate, local_heads, group_count)
    return finish(signal_c, prepared, skip_gain, local_heads, group_count)


def solution(mesh):
    chain_count, head_count = mesh.devices.shape
    halves = 2 if head_count % 2 == 0 else 1
    split_mesh = jax.sharding.Mesh(
        mesh.devices.reshape(chain_count, halves, head_count // halves), ("chain", "half", LANE)
    )
    rows = P(("chain", "half", LANE), None)
    return jax.shard_map(
        shards,
        mesh=split_mesh,
        in_specs=(rows, rows, rows, rows, P(), P()),
        out_specs=rows,
        check_vma=False,
    )
```

```python
import jax
import jax.numpy as jnp
from jax import lax
from jax.sharding import PartitionSpec as P

HEADS = 256
CHANNEL_WIDTH = 64
SSTATE = 256
HEAD_GROUPS = 8
BLOCK = 256


SEQ = ("chain", "half")
LANE = "lane"


def from_behind(array, axis, by):
    size = lax.psum(1, axis)
    pairs = [(i, i + by) for i in range(size) if 0 <= i + by < size]
    return lax.ppermute(array, axis, pairs)


def prepare(input_c, output_c, step_c, decay_rate, local_heads, group_count):
    chain_rows = input_c.shape[0]
    blocks = chain_rows // BLOCK
    per_group = local_heads // group_count
    head_start = lax.axis_index(LANE) * local_heads
    head_rates = lax.dynamic_slice_in_dim(decay_rate, head_start, local_heads)
    step_rate = step_c.astype(jnp.float32).reshape(blocks, BLOCK, local_heads)
    cumul = jnp.cumsum(-head_rates * step_rate, axis=1)
    input_groups = input_c.reshape(blocks, BLOCK, group_count, SSTATE)
    output_groups = output_c.reshape(blocks, BLOCK, group_count, SSTATE)
    causal = jnp.arange(BLOCK)[:, None] >= jnp.arange(BLOCK)[None, :]

    def block_weights(pieces):
        cumul_k, step_k, input_k, output_k = pieces
        scores = jnp.einsum("tgn,sgn->gts", output_k, input_k, preferred_element_type=jnp.float32)
        cumul_heads = cumul_k.T.reshape(group_count, per_group, BLOCK)
        differ = jnp.where(causal, cumul_heads[:, :, :, None] - cumul_heads[:, :, None, :], 0.0)
        decays = jnp.where(causal, jnp.exp(differ), 0.0)
        step_heads = step_k.T.reshape(group_count, per_group, 1, BLOCK)
        weights = decays * scores[:, None] * step_heads
        return weights.astype(jnp.bfloat16).reshape(local_heads, BLOCK, BLOCK)

    weights = lax.map(block_weights, (cumul, step_rate, input_groups, output_groups))
    return (step_rate, cumul, input_groups, output_groups, weights)


def finish(signal_c, prepared, skip_gain, local_heads, group_count):
    step_rate, cumul, input_groups, output_groups, weights = prepared
    blocks = cumul.shape[0]
    per_group = local_heads // group_count
    values = signal_c.reshape(blocks, BLOCK, local_heads, CHANNEL_WIDTH)
    values_wide = values.astype(jnp.float32)
    within = jnp.einsum("khts,kshp->kthp", weights, values, preferred_element_type=jnp.float32)
    to_end = jnp.exp(cumul[:, -1:, :] - cumul) * step_rate
    update = (to_end[..., None] * values_wide).astype(jnp.bfloat16)
    update = update.reshape(blocks, BLOCK, group_count, per_group, CHANNEL_WIDTH)
    fresh_state = jnp.einsum(
        "ksgjp,ksgn->kgjpn", update, input_groups, preferred_element_type=jnp.float32
    )
    fresh_state = fresh_state.reshape(blocks, local_heads, CHANNEL_WIDTH, SSTATE)
    block_ends = cumul[:, -1, :]

    def carry_step(carry_state, pieces):
        block_end, fresh_block = pieces
        return (jnp.exp(block_end)[:, None, None] * carry_state + fresh_block, carry_state)

    empty_state = jnp.zeros((local_heads, CHANNEL_WIDTH, SSTATE), jnp.float32)
    final_state, starts = lax.scan(carry_step, empty_state, (block_ends, fresh_state))
    before = jnp.cumsum(block_ends, axis=0) - block_ends
    totals = jnp.sum(block_ends, axis=0)
    chain_len = lax.axis_size("chain")
    half_count = lax.axis_size("half")
    part = local_heads // half_count
    half = lax.axis_index("half")

    def pack(decay, state):
        rows = state.shape[0] * CHANNEL_WIDTH
        high = decay.astype(jnp.bfloat16)
        low = (decay - high.astype(jnp.float32)).astype(jnp.bfloat16)
        decay_rows = jnp.broadcast_to(jnp.stack([high, low])[:, None, :], (2, 8, decay.shape[0]))
        decay_rows = jnp.pad(decay_rows.reshape(16, -1), ((0, 0), (0, SSTATE - decay.shape[0])))
        wire = state.reshape(rows, SSTATE).astype(jnp.bfloat16)
        return jnp.concatenate([wire, decay_rows], axis=0)

    def unpack(packed, heads, decays):
        rows = heads * CHANNEL_WIDTH
        state = packed[:rows].reshape(heads, CHANNEL_WIDTH, SSTATE).astype(jnp.float32)
        decay = packed[rows, :decays].astype(jnp.float32) + packed[rows + 8, :decays].astype(
            jnp.float32
        )
        return decay, state

    def heads_of(array, which):
        return lax.dynamic_slice_in_dim(array, which * part, part)

    def swap(array):
        return lax.ppermute(array, "half", [(0, 1), (1, 0)])

    own_decay = jnp.exp(totals)
    if half_count == 2:
        sent = pack(own_decay, heads_of(final_state, 1 - half))
        other_decay, other_state = unpack(swap(sent), part, local_heads)
        mine_state = heads_of(final_state, half)
        first = half == 0
        first_decay = jnp.where(first, own_decay, other_decay)
        second_decay = jnp.where(first, other_decay, own_decay)
        first_state = jnp.where(first, mine_state, other_state)
        second_state = jnp.where(first, other_state, mine_state)
        link_decay = heads_of(first_decay * second_decay, half)
        link_state = heads_of(second_decay, half)[:, None, None] * first_state + second_state
    else:
        link_decay, link_state = own_decay, final_state

    got_decay, got_state = unpack(
        from_behind(pack(link_decay, link_state), "chain", 1), part, part
    )
    span_decay = got_decay * link_decay
    span_state = link_decay[:, None, None] * got_state + link_state
    incoming_state = got_state
    incoming_decay = got_decay
    shift = 2
    while shift < chain_len:
        got_decay, got_state = unpack(
            from_behind(pack(span_decay, span_state), "chain", shift), part, part
        )
        incoming_state = incoming_decay[:, None, None] * got_state + incoming_state
        incoming_decay = incoming_decay * got_decay
        if 2 * shift < chain_len:
            span_state = span_decay[:, None, None] * got_state + span_state
            span_decay = span_decay * got_decay
        shift *= 2

    if half_count == 2:
        into_second = heads_of(first_decay, half)[:, None, None] * incoming_state + first_state
        mine_start = jnp.where(first, incoming_state, into_second)
        other_start = swap(
            jnp.where(first, into_second, incoming_state).astype(jnp.bfloat16)
        ).astype(jnp.float32)
        incoming_state = jnp.where(
            first,
            jnp.concatenate([mine_start, other_start], axis=0),
            jnp.concatenate([other_start, mine_start], axis=0),
        )
    starts = starts + jnp.exp(before)[:, :, None, None] * incoming_state
    rounded = starts.astype(jnp.bfloat16).reshape(
        blocks, group_count, per_group, CHANNEL_WIDTH, SSTATE
    )
    carried = jnp.einsum(
        "ktgn,kgjpn->ktgjp", output_groups, rounded, preferred_element_type=jnp.float32
    )
    carried = carried.reshape(blocks, BLOCK, local_heads, CHANNEL_WIDTH) * jnp.exp(cumul)[..., None]
    head_start = lax.axis_index(LANE) * local_heads
    gain_heads = lax.dynamic_slice_in_dim(skip_gain, head_start, local_heads)
    result = (within + carried + gain_heads[:, None] * values_wide).astype(jnp.bfloat16)
    head_count = lax.axis_size(LANE)
    result = result.reshape(head_count, -1, local_heads * CHANNEL_WIDTH)
    lane = lax.axis_index(LANE)
    width = result.shape[2]
    output = jnp.zeros((result.shape[1], head_count * width), result.dtype)
    for shift in range(head_count):
        piece = lax.dynamic_index_in_dim(result, (lane + shift) % head_count, keepdims=False)
        if shift:
            pairs = [(i, (i + shift) % head_count) for i in range(head_count)]
            piece = lax.ppermute(piece, LANE, pairs)
        source = (lane - shift) % head_count
        output = lax.dynamic_update_slice_in_dim(output, piece, source * width, axis=1)
    return output


def shards(signal, input_map, output_map, step_size, decay_rate, skip_gain):
    head_count = lax.axis_size(LANE)
    local_heads = HEADS // head_count
    group_heads = HEADS // HEAD_GROUPS
    group_count = max(1, local_heads // group_heads)
    copies = max(1, group_heads // local_heads)
    row_count = signal.shape[0]
    input_rep = jnp.repeat(
        input_map.reshape(row_count, HEAD_GROUPS, SSTATE), copies, axis=1
    ).reshape(row_count, -1)
    output_rep = jnp.repeat(
        output_map.reshape(row_count, HEAD_GROUPS, SSTATE), copies, axis=1
    ).reshape(row_count, -1)
    per_lane = [input_rep.shape[1] // head_count, output_rep.shape[1] // head_count]
    per_lane.append(step_size.shape[1] // head_count)
    side = jnp.concatenate(
        [
            input_rep.reshape(row_count, head_count, per_lane[0]),
            output_rep.reshape(row_count, head_count, per_lane[1]),
            step_size.reshape(row_count, head_count, per_lane[2]),
        ],
        axis=2,
    )
    side = lax.all_to_all(side, LANE, split_axis=1, concat_axis=0, tiled=True)
    side = side.reshape(side.shape[0], -1)
    input_c = side[:, : per_lane[0]]
    output_c = side[:, per_lane[0] : per_lane[0] + per_lane[1]]
    step_c = side[:, per_lane[0] + per_lane[1] :]
    signal_c = lax.all_to_all(signal, LANE, split_axis=1, concat_axis=0, tiled=True)
    prepared = prepare(input_c, output_c, step_c, decay_rate, local_heads, group_count)
    return finish(signal_c, prepared, skip_gain, local_heads, group_count)


def solution(mesh):
    chain_count, head_count = mesh.devices.shape
    halves = 2 if head_count % 2 == 0 else 1
    split_mesh = jax.sharding.Mesh(
        mesh.devices.reshape(chain_count, halves, head_count // halves), ("chain", "half", LANE)
    )
    rows = P(("chain", "half", LANE), None)
    return jax.shard_map(
        shards,
        mesh=split_mesh,
        in_specs=(rows, rows, rows, rows, P(), P()),
        out_specs=rows,
        check_vma=False,
    )
```

```python
import jax
import jax.numpy as jnp
from jax import lax
from jax.sharding import PartitionSpec as P

HEADS = 256
CHANNEL_WIDTH = 64
SSTATE = 256
HEAD_GROUPS = 8
BLOCK = 256


SEQ = ("chain", "half")
LANE = "lane"


def from_behind(array, axis, by):
    size = lax.psum(1, axis)
    pairs = [(i, i + by) for i in range(size) if 0 <= i + by < size]
    return lax.ppermute(array, axis, pairs)


def prepare(input_c, output_c, step_c, decay_rate, local_heads, group_count):
    chain_rows = input_c.shape[0]
    blocks = chain_rows // BLOCK
    per_group = local_heads // group_count
    head_start = lax.axis_index(LANE) * local_heads
    head_rates = lax.dynamic_slice_in_dim(decay_rate, head_start, local_heads)
    step_rate = step_c.astype(jnp.float32).reshape(blocks, BLOCK, local_heads)
    cumul = jnp.cumsum(-head_rates * step_rate, axis=1)
    input_groups = input_c.reshape(blocks, BLOCK, group_count, SSTATE)
    output_groups = output_c.reshape(blocks, BLOCK, group_count, SSTATE)
    causal = jnp.arange(BLOCK)[:, None] >= jnp.arange(BLOCK)[None, :]

    def block_weights(pieces):
        cumul_k, step_k, input_k, output_k = pieces
        scores = jnp.einsum("tgn,sgn->gts", output_k, input_k, preferred_element_type=jnp.float32)
        cumul_heads = cumul_k.T.reshape(group_count, per_group, BLOCK)
        differ = jnp.where(causal, cumul_heads[:, :, :, None] - cumul_heads[:, :, None, :], 0.0)
        decays = jnp.where(causal, jnp.exp(differ), 0.0)
        step_heads = step_k.T.reshape(group_count, per_group, 1, BLOCK)
        weights = decays * scores[:, None] * step_heads
        return weights.astype(jnp.bfloat16).reshape(local_heads, BLOCK, BLOCK)

    weights = lax.map(block_weights, (cumul, step_rate, input_groups, output_groups))
    return (step_rate, cumul, input_groups, output_groups, weights)


def finish(signal_c, prepared, skip_gain, local_heads, group_count):
    step_rate, cumul, input_groups, output_groups, weights = prepared
    blocks = cumul.shape[0]
    per_group = local_heads // group_count
    values = signal_c.reshape(blocks, BLOCK, local_heads, CHANNEL_WIDTH)
    values_wide = values.astype(jnp.float32)
    within = jnp.einsum("khts,kshp->kthp", weights, values, preferred_element_type=jnp.float32)
    to_end = jnp.exp(cumul[:, -1:, :] - cumul) * step_rate
    update = (to_end[..., None] * values_wide).astype(jnp.bfloat16)
    update = update.reshape(blocks, BLOCK, group_count, per_group, CHANNEL_WIDTH)
    fresh_state = jnp.einsum(
        "ksgjp,ksgn->kgjpn", update, input_groups, preferred_element_type=jnp.float32
    )
    fresh_state = fresh_state.reshape(blocks, local_heads, CHANNEL_WIDTH, SSTATE)
    block_ends = cumul[:, -1, :]

    order = jnp.arange(blocks)
    later = order[:, None] > order[None, :]
    after_sum = jnp.sum(jnp.where(later[:, :, None], block_ends[:, None, :], 0.0), axis=0)
    final_state = jnp.sum(jnp.exp(after_sum)[:, :, None, None] * fresh_state, axis=0)
    between = (order[None, :, None] > order[None, None, :]) & (order[:, None, None] > order[None, None, :])
    between = between & (order[None, :, None] < order[:, None, None])
    gap_sum = jnp.einsum("kij,ih->kjh", between.astype(jnp.float32), block_ends)
    carry_weight = jnp.where(later[:, :, None], jnp.exp(gap_sum), 0.0)
    starts = jnp.sum(carry_weight[:, :, :, None, None] * fresh_state[None], axis=1)
    before = jnp.cumsum(block_ends, axis=0) - block_ends
    totals = jnp.sum(block_ends, axis=0)
    chain_len = lax.axis_size("chain")
    half_count = lax.axis_size("half")
    part = local_heads // half_count
    half = lax.axis_index("half")

    def pack(decay, state):
        rows = state.shape[0] * CHANNEL_WIDTH
        high = decay.astype(jnp.bfloat16)
        low = (decay - high.astype(jnp.float32)).astype(jnp.bfloat16)
        decay_rows = jnp.broadcast_to(jnp.stack([high, low])[:, None, :], (2, 8, decay.shape[0]))
        decay_rows = jnp.pad(decay_rows.reshape(16, -1), ((0, 0), (0, SSTATE - decay.shape[0])))
        wire = state.reshape(rows, SSTATE).astype(jnp.bfloat16)
        return jnp.concatenate([wire, decay_rows], axis=0)

    def unpack(packed, heads, decays):
        rows = heads * CHANNEL_WIDTH
        state = packed[:rows].reshape(heads, CHANNEL_WIDTH, SSTATE).astype(jnp.float32)
        decay = packed[rows, :decays].astype(jnp.float32) + packed[rows + 8, :decays].astype(
            jnp.float32
        )
        return decay, state

    def heads_of(array, which):
        return lax.dynamic_slice_in_dim(array, which * part, part)

    def swap(array):
        return lax.ppermute(array, "half", [(0, 1), (1, 0)])

    own_decay = jnp.exp(totals)
    if half_count == 2:
        sent = pack(own_decay, heads_of(final_state, 1 - half))
        other_decay, other_state = unpack(swap(sent), part, local_heads)
        mine_state = heads_of(final_state, half)
        first = half == 0
        first_decay = jnp.where(first, own_decay, other_decay)
        second_decay = jnp.where(first, other_decay, own_decay)
        first_state = jnp.where(first, mine_state, other_state)
        second_state = jnp.where(first, other_state, mine_state)
        link_decay = heads_of(first_decay * second_decay, half)
        link_state = heads_of(second_decay, half)[:, None, None] * first_state + second_state
    else:
        link_decay, link_state = own_decay, final_state

    got_decay, got_state = unpack(
        from_behind(pack(link_decay, link_state), "chain", 1), part, part
    )
    span_decay = got_decay * link_decay
    span_state = link_decay[:, None, None] * got_state + link_state
    incoming_state = got_state
    incoming_decay = got_decay
    shift = 2
    while shift < chain_len:
        got_decay, got_state = unpack(
            from_behind(pack(span_decay, span_state), "chain", shift), part, part
        )
        incoming_state = incoming_decay[:, None, None] * got_state + incoming_state
        incoming_decay = incoming_decay * got_decay
        if 2 * shift < chain_len:
            span_state = span_decay[:, None, None] * got_state + span_state
            span_decay = span_decay * got_decay
        shift *= 2

    if half_count == 2:
        into_second = heads_of(first_decay, half)[:, None, None] * incoming_state + first_state
        mine_start = jnp.where(first, incoming_state, into_second)
        other_start = swap(
            jnp.where(first, into_second, incoming_state).astype(jnp.bfloat16)
        ).astype(jnp.float32)
        incoming_state = jnp.where(
            first,
            jnp.concatenate([mine_start, other_start], axis=0),
            jnp.concatenate([other_start, mine_start], axis=0),
        )
    starts = starts + jnp.exp(before)[:, :, None, None] * incoming_state
    rounded = starts.astype(jnp.bfloat16).reshape(
        blocks, group_count, per_group, CHANNEL_WIDTH, SSTATE
    )
    carried = jnp.einsum(
        "ktgn,kgjpn->ktgjp", output_groups, rounded, preferred_element_type=jnp.float32
    )
    carried = carried.reshape(blocks, BLOCK, local_heads, CHANNEL_WIDTH) * jnp.exp(cumul)[..., None]
    head_start = lax.axis_index(LANE) * local_heads
    gain_heads = lax.dynamic_slice_in_dim(skip_gain, head_start, local_heads)
    result = (within + carried + gain_heads[:, None] * values_wide).astype(jnp.bfloat16)
    head_count = lax.axis_size(LANE)
    result = result.reshape(head_count, -1, local_heads * CHANNEL_WIDTH).transpose(1, 0, 2)
    result = lax.all_to_all(result, LANE, split_axis=1, concat_axis=1, tiled=True)
    return result.reshape(result.shape[0], -1)


def shards(signal, input_map, output_map, step_size, decay_rate, skip_gain):
    head_count = lax.axis_size(LANE)
    local_heads = HEADS // head_count
    group_heads = HEADS // HEAD_GROUPS
    group_count = max(1, local_heads // group_heads)
    copies = max(1, group_heads // local_heads)
    row_count = signal.shape[0]
    input_rep = jnp.repeat(
        input_map.reshape(row_count, HEAD_GROUPS, SSTATE), copies, axis=1
    ).reshape(row_count, -1)
    output_rep = jnp.repeat(
        output_map.reshape(row_count, HEAD_GROUPS, SSTATE), copies, axis=1
    ).reshape(row_count, -1)
    per_lane = [input_rep.shape[1] // head_count, output_rep.shape[1] // head_count]
    per_lane.append(step_size.shape[1] // head_count)
    side = jnp.concatenate(
        [
            input_rep.reshape(row_count, head_count, per_lane[0]),
            output_rep.reshape(row_count, head_count, per_lane[1]),
            step_size.reshape(row_count, head_count, per_lane[2]),
        ],
        axis=2,
    )
    side = lax.all_to_all(side, LANE, split_axis=1, concat_axis=0, tiled=True)
    side = side.reshape(side.shape[0], -1)
    input_c = side[:, : per_lane[0]]
    output_c = side[:, per_lane[0] : per_lane[0] + per_lane[1]]
    step_c = side[:, per_lane[0] + per_lane[1] :]
    signal_c = lax.all_to_all(signal, LANE, split_axis=1, concat_axis=0, tiled=True)
    prepared = prepare(input_c, output_c, step_c, decay_rate, local_heads, group_count)
    return finish(signal_c, prepared, skip_gain, local_heads, group_count)


def solution(mesh):
    chain_count, head_count = mesh.devices.shape
    halves = 2 if head_count % 2 == 0 else 1
    split_mesh = jax.sharding.Mesh(
        mesh.devices.reshape(chain_count, halves, head_count // halves), ("chain", "half", LANE)
    )
    rows = P(("chain", "half", LANE), None)
    return jax.shard_map(
        shards,
        mesh=split_mesh,
        in_specs=(rows, rows, rows, rows, P(), P()),
        out_specs=rows,
        check_vma=False,
    )
```

```python
import jax
import jax.numpy as jnp
from jax import lax
from jax.sharding import PartitionSpec as P

HEADS = 256
CHANNEL_WIDTH = 64
SSTATE = 256
HEAD_GROUPS = 8
BLOCK = 256


SEQ = ("chain", "half")
LANE = "lane"


def from_behind(array, axis, by):
    size = lax.psum(1, axis)
    pairs = [(i, i + by) for i in range(size) if 0 <= i + by < size]
    return lax.ppermute(array, axis, pairs)


def prepare(input_c, output_c, step_c, decay_rate, local_heads, group_count):
    chain_rows = input_c.shape[0]
    blocks = chain_rows // BLOCK
    per_group = local_heads // group_count
    head_start = lax.axis_index(LANE) * local_heads
    head_rates = lax.dynamic_slice_in_dim(decay_rate, head_start, local_heads)
    step_rate = step_c.astype(jnp.float32).reshape(blocks, BLOCK, local_heads)
    cumul = jnp.cumsum(-head_rates * step_rate, axis=1)
    input_groups = input_c.reshape(blocks, BLOCK, group_count, SSTATE)
    output_groups = output_c.reshape(blocks, BLOCK, group_count, SSTATE)
    causal = jnp.arange(BLOCK)[:, None] >= jnp.arange(BLOCK)[None, :]

    def block_weights(pieces):
        cumul_k, step_k, input_k, output_k = pieces
        scores = jnp.einsum("tgn,sgn->gts", output_k, input_k, preferred_element_type=jnp.float32)
        cumul_heads = cumul_k.T.reshape(group_count, per_group, BLOCK)
        differ = jnp.where(causal, cumul_heads[:, :, :, None] - cumul_heads[:, :, None, :], 0.0)
        decays = jnp.where(causal, jnp.exp(differ), 0.0)
        step_heads = step_k.T.reshape(group_count, per_group, 1, BLOCK)
        weights = decays * scores[:, None] * step_heads
        return weights.astype(jnp.bfloat16).reshape(local_heads, BLOCK, BLOCK)

    weights = lax.map(block_weights, (cumul, step_rate, input_groups, output_groups))
    return (step_rate, cumul, input_groups, output_groups, weights)


def finish(signal_c, prepared, skip_gain, local_heads, group_count):
    step_rate, cumul, input_groups, output_groups, weights = prepared
    blocks = cumul.shape[0]
    per_group = local_heads // group_count
    values = signal_c.reshape(blocks, BLOCK, local_heads, CHANNEL_WIDTH)
    values_wide = values.astype(jnp.float32)
    within = jnp.einsum("khts,kshp->kthp", weights, values, preferred_element_type=jnp.float32)
    to_end = jnp.exp(cumul[:, -1:, :] - cumul) * step_rate
    update = (to_end[..., None] * values_wide).astype(jnp.bfloat16)
    update = update.reshape(blocks, BLOCK, group_count, per_group, CHANNEL_WIDTH)
    fresh_state = jnp.einsum(
        "ksgjp,ksgn->kgjpn", update, input_groups, preferred_element_type=jnp.float32
    )
    fresh_state = fresh_state.reshape(blocks, local_heads, CHANNEL_WIDTH, SSTATE)
    block_ends = cumul[:, -1, :]

    def carry_step(carry_state, pieces):
        block_end, fresh_block = pieces
        return (jnp.exp(block_end)[:, None, None] * carry_state + fresh_block, carry_state)

    empty_state = jnp.zeros((local_heads, CHANNEL_WIDTH, SSTATE), jnp.float32)
    final_state, starts = lax.scan(carry_step, empty_state, (block_ends, fresh_state))
    before = jnp.cumsum(block_ends, axis=0) - block_ends
    totals = jnp.sum(block_ends, axis=0)
    chain_len = lax.axis_size("chain")
    half_count = lax.axis_size("half")
    part = local_heads // half_count
    half = lax.axis_index("half")

    def pack(decay, state):
        rows = state.shape[0] * CHANNEL_WIDTH
        high = decay.astype(jnp.bfloat16)
        low = (decay - high.astype(jnp.float32)).astype(jnp.bfloat16)
        decay_rows = jnp.broadcast_to(jnp.stack([high, low])[:, None, :], (2, 8, decay.shape[0]))
        decay_rows = jnp.pad(decay_rows.reshape(16, -1), ((0, 0), (0, SSTATE - decay.shape[0])))
        wire = state.reshape(rows, SSTATE).astype(jnp.bfloat16)
        return jnp.concatenate([wire, decay_rows], axis=0)

    def unpack(packed, heads, decays):
        rows = heads * CHANNEL_WIDTH
        state = packed[:rows].reshape(heads, CHANNEL_WIDTH, SSTATE).astype(jnp.float32)
        decay = packed[rows, :decays].astype(jnp.float32) + packed[rows + 8, :decays].astype(
            jnp.float32
        )
        return decay, state

    def heads_of(array, which):
        return lax.dynamic_slice_in_dim(array, which * part, part)

    def swap(array):
        return lax.ppermute(array, "half", [(0, 1), (1, 0)])

    own_decay = jnp.exp(totals)
    if half_count == 2:
        sent = pack(own_decay, heads_of(final_state, 1 - half))
        other_decay, other_state = unpack(swap(sent), part, local_heads)
        mine_state = heads_of(final_state, half)
        first = half == 0
        first_decay = jnp.where(first, own_decay, other_decay)
        second_decay = jnp.where(first, other_decay, own_decay)
        first_state = jnp.where(first, mine_state, other_state)
        second_state = jnp.where(first, other_state, mine_state)
        link_decay = heads_of(first_decay * second_decay, half)
        link_state = heads_of(second_decay, half)[:, None, None] * first_state + second_state
    else:
        link_decay, link_state = own_decay, final_state

    got_decay, got_state = unpack(
        from_behind(pack(link_decay, link_state), "chain", 1), part, part
    )
    span_decay = got_decay * link_decay
    span_state = link_decay[:, None, None] * got_state + link_state
    incoming_state = got_state
    incoming_decay = got_decay
    shift = 2
    while shift < chain_len:
        got_decay, got_state = unpack(
            from_behind(pack(span_decay, span_state), "chain", shift), part, part
        )
        incoming_state = incoming_decay[:, None, None] * got_state + incoming_state
        incoming_decay = incoming_decay * got_decay
        if 2 * shift < chain_len:
            span_state = span_decay[:, None, None] * got_state + span_state
            span_decay = span_decay * got_decay
        shift *= 2

    if half_count == 2:
        into_second = heads_of(first_decay, half)[:, None, None] * incoming_state + first_state
        mine_start = jnp.where(first, incoming_state, into_second)
        other_start = swap(
            jnp.where(first, into_second, incoming_state).astype(jnp.bfloat16)
        ).astype(jnp.float32)
        incoming_state = jnp.where(
            first,
            jnp.concatenate([mine_start, other_start], axis=0),
            jnp.concatenate([other_start, mine_start], axis=0),
        )
    starts = starts + jnp.exp(before)[:, :, None, None] * incoming_state
    rounded = starts.astype(jnp.bfloat16).reshape(
        blocks, group_count, per_group, CHANNEL_WIDTH, SSTATE
    )
    carried = jnp.einsum(
        "ktgn,kgjpn->ktgjp", output_groups, rounded, preferred_element_type=jnp.float32
    )
    carried = carried.reshape(blocks, BLOCK, local_heads, CHANNEL_WIDTH) * jnp.exp(cumul)[..., None]
    head_start = lax.axis_index(LANE) * local_heads
    gain_heads = lax.dynamic_slice_in_dim(skip_gain, head_start, local_heads)
    result = (within + carried + gain_heads[:, None] * values_wide).astype(jnp.bfloat16)
    head_count = lax.axis_size(LANE)
    parts = []
    for piece in jnp.split(result, 2, axis=2):
        piece = piece.reshape(head_count, -1, piece.shape[2] * CHANNEL_WIDTH).transpose(1, 0, 2)
        parts.append(lax.all_to_all(piece, LANE, split_axis=1, concat_axis=1, tiled=True))
    result = jnp.concatenate(parts, axis=2)
    return result.reshape(result.shape[0], -1)


def shards(signal, input_map, output_map, step_size, decay_rate, skip_gain):
    head_count = lax.axis_size(LANE)
    local_heads = HEADS // head_count
    group_heads = HEADS // HEAD_GROUPS
    group_count = max(1, local_heads // group_heads)
    copies = max(1, group_heads // local_heads)
    row_count = signal.shape[0]
    input_rep = jnp.repeat(
        input_map.reshape(row_count, HEAD_GROUPS, SSTATE), copies, axis=1
    ).reshape(row_count, -1)
    output_rep = jnp.repeat(
        output_map.reshape(row_count, HEAD_GROUPS, SSTATE), copies, axis=1
    ).reshape(row_count, -1)
    per_lane = [input_rep.shape[1] // head_count, output_rep.shape[1] // head_count]
    per_lane.append(step_size.shape[1] // head_count)
    side = jnp.concatenate(
        [
            input_rep.reshape(row_count, head_count, per_lane[0]),
            output_rep.reshape(row_count, head_count, per_lane[1]),
            step_size.reshape(row_count, head_count, per_lane[2]),
        ],
        axis=2,
    )
    side = lax.all_to_all(side, LANE, split_axis=1, concat_axis=0, tiled=True)
    side = side.reshape(side.shape[0], -1)
    input_c = side[:, : per_lane[0]]
    output_c = side[:, per_lane[0] : per_lane[0] + per_lane[1]]
    step_c = side[:, per_lane[0] + per_lane[1] :]
    signal_c = lax.all_to_all(signal, LANE, split_axis=1, concat_axis=0, tiled=True)
    prepared = prepare(input_c, output_c, step_c, decay_rate, local_heads, group_count)
    return finish(signal_c, prepared, skip_gain, local_heads, group_count)


def solution(mesh):
    chain_count, head_count = mesh.devices.shape
    halves = 2 if head_count % 2 == 0 else 1
    split_mesh = jax.sharding.Mesh(
        mesh.devices.reshape(chain_count, halves, head_count // halves), ("chain", "half", LANE)
    )
    rows = P(("chain", "half", LANE), None)
    return jax.shard_map(
        shards,
        mesh=split_mesh,
        in_specs=(rows, rows, rows, rows, P(), P()),
        out_specs=rows,
        check_vma=False,
    )
```
